128 devices in a mesh: gx: 32 (over x, z, core), dev: 4 (over y).
Axes of the slice: x: 4, y: 4, z: 4, core: 2. Of those that a mesh axis runs over, the one named last changes fastest.
Arguments:
- densities: float32 [8, 192, 256, 256], P('dev', 'gx'), may hold values from 0.05 to 2000, as said below
- raw_weights: float32 [8], replicated, may hold values from 0.5 to 2
Outputs:
- barycenter: float32 [192, 256, 256], P('gx')
- scalings: float32 [8, 192, 256, 256], P('dev', 'gx')
The draws below stay inside these ranges and needn't reach their ends.
Inputs may be any that keep to these rules, and one draw needn't show every extreme that they name: `densities`: every entry is positive.
All inputs are finite; a program needn't handle non-finite values.
Results may differ from the reference program's by a relative error of at most 0.000043.
Values sent between devices are 32-bit elements; how exact they have to be, the bound alone decides.
No kernel may reach another device: no remote copies, remote signals or barrier semaphores. Data moves between devices by JAX's collectives and lax.ppermute only.
A program may use at most 64 MiB of HBM per device.

```python
import math
import jax
import jax.numpy as jnp
import numpy as np
from jax import lax

K = 8
ITERS = 2
NY = 256
NZ = 256
NX = 192


def draw_densities(key, part):
    keys = jax.random.split(key, 3)
    shape = (K, NX, NY, NZ)
    position = jnp.arange(NX).astype(jnp.float32)
    rise = 1.0 + 2.0 * position / max(NX - 1, 1)
    plane = jnp.exp(jax.random.uniform(keys[1], (K, NX, 1, 1), jnp.float32, 0.0, math.log(10.0)))
    cell = jnp.exp(jax.random.uniform(keys[0], shape, jnp.float32, -1.6, 1.6))
    row = jnp.exp(jax.random.uniform(keys[2], (K, 1, NY, 1), jnp.float32, 0.0, math.log(10.0)))
    return cell * plane * row * rise[None, :, None, None]


def setup_inputs(seed: int = 0) -> dict:
    key_of = jax.random.split(jax.random.key(seed), 3)
    return {
        "densities": draw_densities(jax.random.fold_in(key_of[2], 71), 0),
        "raw_weights": jnp.clip(jnp.exp(jax.random.uniform(key_of[1], (K,), jnp.float32, math.log(0.5), math.log(2.0))), 0.5, 2.0),
    }


gauss_raw = np.exp(-(np.arange(-6, 7) ** 2) / 12.5)
gauss_taps = [float(value) for value in gauss_raw / gauss_raw.sum()]


def smooth_along(field, axis):
    length = field.shape[axis]
    reach = len(gauss_taps) // 2
    widths = [(0, 0)] * field.ndim
    widths[axis] = (reach, reach)
    padded = jnp.pad(field, widths)
    total = gauss_taps[0] * lax.slice_in_dim(padded, 0, length, axis=axis)
    for index in range(1, len(gauss_taps)):
        total = total + gauss_taps[index] * lax.slice_in_dim(padded, index, index + length, axis=axis)
    return total


def heat_blur(field):
    return smooth_along(smooth_along(smooth_along(field, 0), 1), 2)


def reference(densities, raw_weights):
    lam = raw_weights / jnp.sum(raw_weights)
    mass = jnp.mean(densities, axis=(1, 2, 3))
    normed = densities / mass[:, None, None, None]
    count = densities.shape[0]
    scal = [jnp.ones(densities.shape[1:], jnp.float32) for index in range(count)]
    barycenter = scal[0]
    for step in range(ITERS):
        logsum = jnp.zeros(densities.shape[1:], jnp.float32)
        dlist = []
        for index in range(count):
            wfield = normed[index] / heat_blur(scal[index])
            dfield = scal[index] * heat_blur(wfield)
            logsum = logsum + lam[index] * jnp.log(dfield)
            dlist.append(dfield)
        barycenter = jnp.exp(logsum)
        scal = [scal[index] * barycenter / dlist[index] for index in range(count)]
    return barycenter, jnp.stack(scal)
```

```python
import jax
import jax.numpy as jnp
import numpy as np
from jax import lax
from jax.sharding import PartitionSpec as P

ITERS = 2


gauss_raw = np.exp(-np.arange(-6, 7) ** 2 / 12.5)
gauss_taps = [float(value) for value in gauss_raw / gauss_raw.sum()]


def padded_2(cells, sides, width):
    for axis, dim in sides:
        count = lax.axis_size(axis)
        ends = count - 1
        head = lax.slice_in_dim(cells, 0, width, axis=dim)
        tail = lax.slice_in_dim(cells, cells.shape[dim] - width, cells.shape[dim], axis=dim)
        cells = jnp.concatenate(
            [
                lax.ppermute(tail, axis, [(i, (i + 1) % count) for i in range(ends)]),
                cells,
                lax.ppermute(head, axis, [((i + 1) % count, i) for i in range(ends)]),
            ],
            axis=dim,
        )
    return cells


def taps_over(padded, axis, length):
    total = gauss_taps[0] * lax.slice_in_dim(padded, 0, length, axis=axis)
    for index in range(1, len(gauss_taps)):
        total = total + gauss_taps[index] * lax.slice_in_dim(
            padded, index, index + length, axis=axis
        )
    return total


def pad_axis(field, axis):
    reach = len(gauss_taps) // 2
    widths = [(0, 0)] * field.ndim
    widths[axis] = (reach, reach)
    return jnp.pad(field, widths)


def heat_blur(field):
    reach = len(gauss_taps) // 2
    planes = field.shape[1]
    padded = padded_2(field, (("gx", 1),), reach)
    along = taps_over(padded, 1, planes)
    along = taps_over(pad_axis(along, 2), 2, along.shape[2])
    return taps_over(pad_axis(along, 3), 3, along.shape[3])


def ones_profile(length):
    reach = len(gauss_taps) // 2
    out = np.zeros(length, np.float32)
    for position in range(length):
        acc = np.float32(0.0)
        for index, tap in enumerate(gauss_taps):
            source = position + index - reach
            if 0 <= source < length:
                acc = acc + np.float32(tap)
        out[position] = acc
    return out


def per_device(densities, raw_weights):
    local_count = densities.shape[0]
    planes = densities.shape[1]
    lam = raw_weights / jnp.sum(raw_weights)
    offset = lax.axis_index("dev") * local_count
    lam_local = lax.dynamic_slice_in_dim(lam, offset, local_count)
    total_planes = planes * lax.axis_size("gx")
    cells = total_planes * densities.shape[2] * densities.shape[3]
    local_sums = jnp.sum(densities, axis=(1, 2, 3))
    mass = lax.psum(local_sums, "gx") / cells
    profile_x = lax.dynamic_slice_in_dim(
        jnp.asarray(ones_profile(total_planes)), lax.axis_index("gx") * planes, planes
    )
    profile_y = jnp.asarray(ones_profile(densities.shape[2]))
    profile_z = jnp.asarray(ones_profile(densities.shape[3]))
    blur_ones = profile_x[:, None, None] * profile_y[None, :, None] * profile_z[None, None, :]
    raw_d = heat_blur(densities / blur_ones[None])
    dfield = raw_d / mass[:, None, None, None]
    partial_log = jnp.sum(lam_local[:, None, None, None] * jnp.log(dfield), axis=0)
    barycenter = jnp.exp(lax.psum(partial_log, "dev"))
    scal = barycenter[None] / dfield
    field = densities / mass[:, None, None, None]
    for step in range(1, ITERS):
        wfield = field / heat_blur(scal)
        dfield = scal * heat_blur(wfield)
        partial_log = jnp.sum(lam_local[:, None, None, None] * jnp.log(dfield), axis=0)
        barycenter = jnp.exp(lax.psum(partial_log, "dev"))
        scal = scal * barycenter[None] / dfield
    return (barycenter, scal)


def solution(mesh):
    in_specs = (P("dev", "gx", None, None), P())
    out_specs = (P("gx", None, None), P("dev", "gx", None, None))
    return jax.shard_map(
        per_device, mesh=mesh, in_specs=in_specs, out_specs=out_specs, check_vma=False
    )
```

```python
import jax
import jax.numpy as jnp
import numpy as np
from jax import lax
from jax.sharding import PartitionSpec as P

ITERS = 2


gauss_raw = np.exp(-np.arange(-6, 7) ** 2 / 12.5)
gauss_taps = [float(value) for value in gauss_raw / gauss_raw.sum()]


def padded_2(cells, sides, width):
    for axis, dim in sides:
        count = lax.axis_size(axis)
        ends = count - 1
        head = lax.slice_in_dim(cells, 0, width, axis=dim)
        tail = lax.slice_in_dim(cells, cells.shape[dim] - width, cells.shape[dim], axis=dim)
        cells = jnp.concatenate(
            [
                lax.ppermute(tail, axis, [(i, (i + 1) % count) for i in range(ends)]),
                cells,
                lax.ppermute(head, axis, [((i + 1) % count, i) for i in range(ends)]),
            ],
            axis=dim,
        )
    return cells


def taps_over(padded, axis, length):
    total = gauss_taps[0] * lax.slice_in_dim(padded, 0, length, axis=axis)
    for index in range(1, len(gauss_taps)):
        total = total + gauss_taps[index] * lax.slice_in_dim(
            padded, index, index + length, axis=axis
        )
    return total


def pad_axis(field, axis):
    reach = len(gauss_taps) // 2
    widths = [(0, 0)] * field.ndim
    widths[axis] = (reach, reach)
    return jnp.pad(field, widths)


def heat_blur(field):
    reach = len(gauss_taps) // 2
    planes = field.shape[1]
    padded = padded_2(field, (("gx", 1),), reach)
    along = taps_over(padded, 1, planes)
    along = taps_over(pad_axis(along, 2), 2, along.shape[2])
    return taps_over(pad_axis(along, 3), 3, along.shape[3])


def ones_profile(length):
    reach = len(gauss_taps) // 2
    out = np.zeros(length, np.float32)
    for position in range(length):
        acc = np.float32(0.0)
        for index, tap in enumerate(gauss_taps):
            source = position + index - reach
            if 0 <= source < length:
                acc = acc + np.float32(tap)
        out[position] = acc
    return out


def per_device(densities, raw_weights):
    local_count = densities.shape[0]
    planes = densities.shape[1]
    lam = raw_weights / jnp.sum(raw_weights)
    offset = lax.axis_index("dev") * local_count
    lam_local = lax.dynamic_slice_in_dim(lam, offset, local_count)
    total_planes = planes * lax.axis_size("gx")
    cells = total_planes * densities.shape[2] * densities.shape[3]
    local_sums = jnp.sum(densities, axis=(1, 2, 3))
    mass = lax.psum(jnp.broadcast_to(local_sums[:, None], (local_sums.shape[0], 8192)), "gx")[:, 0] / cells
    profile_x = lax.dynamic_slice_in_dim(
        jnp.asarray(ones_profile(total_planes)), lax.axis_index("gx") * planes, planes
    )
    profile_y = jnp.asarray(ones_profile(densities.shape[2]))
    profile_z = jnp.asarray(ones_profile(densities.shape[3]))
    blur_ones = profile_x[:, None, None] * profile_y[None, :, None] * profile_z[None, None, :]
    raw_d = heat_blur(densities / blur_ones[None])
    dfield = raw_d / mass[:, None, None, None]
    partial_log = jnp.sum(lam_local[:, None, None, None] * jnp.log(dfield), axis=0)
    barycenter = jnp.exp(lax.psum(partial_log, "dev"))
    scal = barycenter[None] / dfield
    field = densities / mass[:, None, None, None]
    for step in range(1, ITERS):
        wfield = field / heat_blur(scal)
        dfield = scal * heat_blur(wfield)
        partial_log = jnp.sum(lam_local[:, None, None, None] * jnp.log(dfield), axis=0)
        barycenter = jnp.exp(lax.psum(partial_log, "dev"))
        scal = scal * barycenter[None] / dfield
    return (barycenter, scal)


def solution(mesh):
    in_specs = (P("dev", "gx", None, None), P())
    out_specs = (P("gx", None, None), P("dev", "gx", None, None))
    return jax.shard_map(
        per_device, mesh=mesh, in_specs=in_specs, out_specs=out_specs, check_vma=False
    )
```

```python
import jax
import jax.numpy as jnp
import numpy as np
from jax import lax
from jax.sharding import PartitionSpec as P

ITERS = 2


gauss_raw = np.exp(-np.arange(-6, 7) ** 2 / 12.5)
gauss_taps = [float(value) for value in gauss_raw / gauss_raw.sum()]


def padded_2(cells, sides, width):
    for axis, dim in sides:
        count = lax.axis_size(axis)
        ends = count - 1
        head = lax.slice_in_dim(cells, 0, width, axis=dim)
        tail = lax.slice_in_dim(cells, cells.shape[dim] - width, cells.shape[dim], axis=dim)
        cells = jnp.concatenate(
            [
                lax.ppermute(tail, axis, [(i, (i + 1) % count) for i in range(ends)]),
                cells,
                lax.ppermute(head, axis, [((i + 1) % count, i) for i in range(ends)]),
            ],
            axis=dim,
        )
    return cells


def taps_over(padded, axis, length):
    total = gauss_taps[0] * lax.slice_in_dim(padded, 0, length, axis=axis)
    for index in range(1, len(gauss_taps)):
        total = total + gauss_taps[index] * lax.slice_in_dim(
            padded, index, index + length, axis=axis
        )
    return total


def pad_axis(field, axis):
    reach = len(gauss_taps) // 2
    widths = [(0, 0)] * field.ndim
    widths[axis] = (reach, reach)
    return jnp.pad(field, widths)


def heat_blur(field):
    reach = len(gauss_taps) // 2
    planes = field.shape[1]
    padded = padded_2(field, (("gx", 1),), reach)
    along = taps_over(padded, 1, planes)
    along = taps_over(pad_axis(along, 2), 2, along.shape[2])
    return taps_over(pad_axis(along, 3), 3, along.shape[3])


def ones_profile(length):
    reach = len(gauss_taps) // 2
    out = np.zeros(length, np.float32)
    for position in range(length):
        acc = np.float32(0.0)
        for index, tap in enumerate(gauss_taps):
            source = position + index - reach
            if 0 <= source < length:
                acc = acc + np.float32(tap)
        out[position] = acc
    return out


def per_device(densities, raw_weights):
    local_count = densities.shape[0]
    planes = densities.shape[1]
    lam = raw_weights / jnp.sum(raw_weights)
    offset = lax.axis_index("dev") * local_count
    lam_local = lax.dynamic_slice_in_dim(lam, offset, local_count)
    total_planes = planes * lax.axis_size("gx")
    cells = total_planes * densities.shape[2] * densities.shape[3]
    local_sums = jnp.sum(densities, axis=(1, 2, 3))
    mass = jnp.sum(lax.all_gather(local_sums, "gx"), axis=0) / cells
    profile_x = lax.dynamic_slice_in_dim(
        jnp.asarray(ones_profile(total_planes)), lax.axis_index("gx") * planes, planes
    )
    profile_y = jnp.asarray(ones_profile(densities.shape[2]))
    profile_z = jnp.asarray(ones_profile(densities.shape[3]))
    blur_ones = profile_x[:, None, None] * profile_y[None, :, None] * profile_z[None, None, :]
    raw_d = heat_blur(densities / blur_ones[None])
    dfield = raw_d / mass[:, None, None, None]
    partial_log = jnp.sum(lam_local[:, None, None, None] * jnp.log(dfield), axis=0)
    barycenter = jnp.exp(lax.psum(partial_log, "dev"))
    scal = barycenter[None] / dfield
    field = densities / mass[:, None, None, None]
    for step in range(1, ITERS):
        wfield = field / heat_blur(scal)
        dfield = scal * heat_blur(wfield)
        partial_log = jnp.sum(lam_local[:, None, None, None] * jnp.log(dfield), axis=0)
        barycenter = jnp.exp(lax.psum(partial_log, "dev"))
        scal = scal * barycenter[None] / dfield
    return (barycenter, scal)


def solution(mesh):
    in_specs = (P("dev", "gx", None, None), P())
    out_specs = (P("gx", None, None), P("dev", "gx", None, None))
    return jax.shard_map(
        per_device, mesh=mesh, in_specs=in_specs, out_specs=out_specs, check_vma=False
    )
```
